128 devices in a mesh: gx: 16 (over y, x_lo, core), gy: 8 (over z, x_hi).
Axes of the slice: x: 4 (x_hi: 2, x_lo: 2; x = x_hi * 2 + x_lo), y: 4, z: 4, core: 2. Of those that a mesh axis runs over, the one named last changes fastest.
Arguments:
- features: bfloat16 [131072, 256], P(('gx', 'gy')), may hold values from -6 to 6
- valid: int32 [131072], P(('gx', 'gy')), may hold values from 0 to 1, as said below
- cotangent: bfloat16 [131072, 256], P(('gx', 'gy')), may hold values from -6 to 6
- gamma: float32 [256], replicated, may hold values from 0.5 to 1.5
- w_qkv: bfloat16 [256, 768], replicated
- w_out: bfloat16 [256, 256], replicated, may hold values from -0.375 to 0.375
Outputs:
- block_out: bfloat16 [131072, 256], P(('gx', 'gy'))
- grad_x: bfloat16 [131072, 256], P(('gx', 'gy'))
- grad_wqkv: float32 [256, 768], replicated
- grad_wout: float32 [256, 256], replicated
- gamma_gradient: float32 [256], replicated
The draws below stay inside these ranges and needn't reach their ends.
Inputs may be any that keep to these rules, and one draw needn't show every extreme that they name: `valid`: the node that takes the first position of each patch in transposed order is occupied.
All inputs are finite; a program needn't handle non-finite values.
Results may differ from the reference program's by a relative error of at most 0.015.
The reference program's roundings to bfloat16 on the way count: a program that leaves them out, or rounds other values in their place, can miss the bound.
Values may be sent and summed in bfloat16 or wider, within the bound.
No kernel may reach another device: no remote copies, remote signals or barrier semaphores. Data moves between devices by JAX's collectives and lax.ppermute only.
A program may use at most 64 MiB of HBM per device.

```python
import jax
import jax.numpy as jnp
from jax import lax

C = 256
HEADS = 16
K = 1024
ROWS = 1024
BLOCK = 8
NODES = 131072
N_GX = 16
N_GY = 8


def draw_valid(key, part):
    count = N_GX * N_GY
    level = jax.random.randint(jax.random.fold_in(key, 11), (count,), 1, 5)
    level = level.at[0].set(4)
    draws = jax.random.randint(jax.random.fold_in(key, 12), (NODES,), 0, 4)
    index = jnp.arange(NODES, dtype=jnp.int32)
    device = index // ROWS
    offset = index % BLOCK
    source = index // BLOCK % count
    target = index // (BLOCK * count)
    moved = (source * count + target) * BLOCK + offset
    first = moved % K == 0
    occupied = jnp.logical_or(draws < level[device], first)
    return jnp.where(occupied, 1, 0).astype(jnp.int32)


def draw_w_qkv(key, part):
    scale = C ** (-0.5)
    full = jax.random.normal(jax.random.fold_in(key, 23), (C, 3 * C), jnp.float32) * scale
    return full.astype(jnp.bfloat16)


def block_levels(own_key, dims, shards, least, high):
    level = 1.0
    for axis_at, blocks in shards:
        heights = jax.random.uniform(jax.random.fold_in(jax.random.fold_in(own_key, 6), axis_at), (blocks,), jnp.float32, least / len(shards), high / len(shards))
        level = level * jnp.repeat(jnp.exp(heights), dims[axis_at] // blocks).reshape((-1,) + (1,) * (len(dims) - 1 - axis_at))
    return level


def centred(own_key, dims, spread, limit, cuts=(), held_as=jnp.bfloat16):
    entries = jax.random.normal(own_key, dims, jnp.float32) * spread
    if len(cuts) > 0:
        entries = block_levels(own_key, dims, cuts, -0.22, 0.18) * entries
    return jnp.clip(entries, min=-limit, max=limit).astype(held_as)


def setup_inputs(seed: int = 0) -> dict:
    splits = jax.random.split(jax.random.key(seed), 7)
    return {
        "features": centred(splits[0], (NODES, C), 1.0, 6.0, ((0, 128),)),
        "valid": draw_valid(jax.random.fold_in(splits[6], 71), 0),
        "cotangent": centred(splits[2], (NODES, C), 1.0, 6.0, ((0, 128),)),
        "gamma": jnp.clip(1.0 + 0.1 * jax.random.normal(splits[3], (C,), jnp.float32), 0.5, 1.5),
        "w_qkv": draw_w_qkv(jax.random.fold_in(splits[6], 71), 0),
        "w_out": centred(splits[5], (C, C), C ** -0.5, 0.375),
    }


def reorder(array, count, block):
    rest = array.shape[1:]
    shaped = array.reshape((count, count, block) + rest)
    return jnp.swapaxes(shaped, 0, 1).reshape(array.shape)

def layer_norm_apply(input_rows, gamma):
    xf = input_rows.astype(jnp.float32)
    centered_input = xf - lax.optimization_barrier(jnp.mean(xf, -1, keepdims=True))
    reciprocal_deviation = lax.rsqrt(lax.optimization_barrier(jnp.mean(centered_input * centered_input, -1, keepdims=True)) + 1e-05)
    normalized_input = centered_input * reciprocal_deviation
    return (normalized_input, reciprocal_deviation, (normalized_input * gamma.astype(jnp.float32)).astype(jnp.bfloat16))

def head_probs(query, keys, keep, scale):
    scores = jnp.dot(query, keys.T, preferred_element_type=jnp.float32) * scale
    scores = jnp.where(keep[None, :], scores, -1e+30)
    expo = jnp.exp(scores - lax.optimization_barrier(jnp.max(scores, -1, keepdims=True)))
    return expo / lax.optimization_barrier(jnp.sum(expo, -1, keepdims=True))

def split_heads(block, heads):
    return block.reshape(block.shape[0], heads, -1).transpose(1, 0, 2)

def join_heads(block):
    return block.transpose(1, 0, 2).reshape(block.shape[1], -1)

def patch_forward(qkv_block, keep, heads):
    width = qkv_block.shape[1] // 3
    scale = (width // heads) ** (-0.5)
    query = split_heads(qkv_block[:, :width], heads)
    keys = split_heads(qkv_block[:, width:2 * width], heads)
    values = split_heads(qkv_block[:, 2 * width:], heads)

    def one_head(parts):
        probs = head_probs(parts[0], parts[1], keep, scale).astype(jnp.bfloat16)
        return jnp.dot(probs, parts[2], preferred_element_type=jnp.float32).astype(jnp.bfloat16)
    return join_heads(lax.map(one_head, (query, keys, values)))

def patch_backward(qkv_block, keep, grad_block, heads):
    width = qkv_block.shape[1] // 3
    scale = (width // heads) ** (-0.5)
    query = split_heads(qkv_block[:, :width], heads)
    keys = split_heads(qkv_block[:, width:2 * width], heads)
    values = split_heads(qkv_block[:, 2 * width:], heads)
    grads = split_heads(grad_block, heads)

    def one_head(parts):
        q_head, k_head, v_head, g_head = parts
        probs = head_probs(q_head, k_head, keep, scale)
        rounded = probs.astype(jnp.bfloat16)
        d_value = jnp.dot(rounded.T, g_head, preferred_element_type=jnp.float32).astype(jnp.bfloat16)
        d_prob = jnp.dot(g_head, v_head.T, preferred_element_type=jnp.float32)
        d_score = (probs * (d_prob - lax.optimization_barrier(jnp.sum(d_prob * probs, -1, keepdims=True))) * scale).astype(jnp.bfloat16)
        d_query = jnp.dot(d_score, k_head, preferred_element_type=jnp.float32).astype(jnp.bfloat16)
        d_key = jnp.dot(d_score.T, q_head, preferred_element_type=jnp.float32).astype(jnp.bfloat16)
        return (d_query, d_key, d_value)
    d_query, d_key, d_value = lax.map(one_head, (query, keys, values, grads))
    return jnp.concatenate([join_heads(d_query), join_heads(d_key), join_heads(d_value)], 1)

def reference(features, valid, cotangent, gamma, w_qkv, w_out):
    count = N_GX * N_GY
    block = NODES // (count * count)
    input_rows = reorder(features, count, block)
    keep = reorder(valid, count, block) > 0
    gt = reorder(cotangent, count, block)
    inverse_root = float(NODES) ** (-0.5)
    normalized_input, reciprocal_deviation, hidden_state = layer_norm_apply(input_rows, gamma)
    qkv = jnp.dot(hidden_state, w_qkv, preferred_element_type=jnp.float32).astype(jnp.bfloat16)
    qkv_p = qkv.reshape(NODES // K, K, 3 * C)
    keep_p = keep.reshape(NODES // K, K)
    attn = lax.map(lambda a: patch_forward(a[0], a[1], HEADS), (qkv_p, keep_p)).reshape(NODES, C)
    y_val = (input_rows.astype(jnp.float32) + jnp.dot(attn, w_out, preferred_element_type=jnp.float32)).astype(jnp.bfloat16)
    grad_wout = jnp.dot(attn.T, gt, preferred_element_type=jnp.float32) * inverse_root
    d_attn = jnp.dot(gt, w_out.T, preferred_element_type=jnp.float32).astype(jnp.bfloat16)
    d_attn_p = d_attn.reshape(NODES // K, K, C)
    d_qkv = lax.map(lambda a: patch_backward(a[0], a[1], a[2], HEADS), (qkv_p, keep_p, d_attn_p)).reshape(NODES, 3 * C)
    grad_wqkv = jnp.dot(hidden_state.T, d_qkv, preferred_element_type=jnp.float32) * inverse_root
    hidden_gradient = jnp.dot(d_qkv, w_qkv.T, preferred_element_type=jnp.float32)
    gamma_gradient = lax.optimization_barrier(jnp.sum(hidden_gradient * normalized_input, 0)) * inverse_root
    scaled_output = hidden_gradient * gamma.astype(jnp.float32)
    norm_gradient = reciprocal_deviation * (scaled_output - lax.optimization_barrier(jnp.mean(scaled_output, -1, keepdims=True)) - normalized_input * lax.optimization_barrier(jnp.mean(scaled_output * normalized_input, -1, keepdims=True)))
    d_x = (gt.astype(jnp.float32) + norm_gradient).astype(jnp.bfloat16)
    return (reorder(y_val, count, block), reorder(d_x, count, block), grad_wqkv, grad_wout, gamma_gradient)
```

```python
import functools

import jax
import jax.numpy as jnp
from jax import lax
from jax.experimental import pallas as pl
from jax.experimental.pallas import tpu as pltpu
from jax.sharding import PartitionSpec as P

HEADS = 16
K = 1024
TQ = 256


def layer_norm_apply(input_rows, gamma):
    xf = input_rows.astype(jnp.float32)
    centered_input = xf - jnp.mean(xf, -1, keepdims=True)
    reciprocal_deviation = lax.rsqrt(
        jnp.mean(centered_input * centered_input, -1, keepdims=True) + 1e-05
    )
    normalized_input = centered_input * reciprocal_deviation
    return (normalized_input, reciprocal_deviation, (normalized_input * gamma).astype(jnp.bfloat16))


def _attn_kernel(qkv_ref, do_ref, keep_ref, o_ref, dqkv_ref, *, scale, n, tq):
    qT = qkv_ref[0]
    kT = qkv_ref[1]
    vT = qkv_ref[2]
    doT = do_ref[...]
    keep = keep_ref[...] > 0.5
    d = qT.shape[0]
    dk_acc = jnp.zeros((d, n), jnp.float32)
    dv_acc = jnp.zeros((d, n), jnp.float32)
    for b in range(n // tq):
        cols = slice(b * tq, (b + 1) * tq)
        qT_b = qT[:, cols]
        doT_b = doT[:, cols]
        q_b = qT_b.T
        do_b = doT_b.T
        s = jnp.dot(q_b, kT, preferred_element_type=jnp.float32) * scale
        s = jnp.where(keep, s, -1e30)
        m = jnp.max(s, -1, keepdims=True)
        e = jnp.exp(s - m)
        l = jnp.sum(e, -1, keepdims=True)
        p = e * (1.0 / l)
        pb = p.astype(jnp.bfloat16)
        o_ref[:, cols] = lax.dot_general(
            vT, pb, (((1,), (1,)), ((), ())), preferred_element_type=jnp.float32
        ).astype(o_ref.dtype)
        dv_acc = dv_acc + jnp.dot(doT_b, pb, preferred_element_type=jnp.float32)
        dp = jnp.dot(do_b, vT, preferred_element_type=jnp.float32)
        rs = jnp.sum(dp * p, -1, keepdims=True)
        ds = (p * (dp - rs) * scale).astype(jnp.bfloat16)
        dqkv_ref[0, :, cols] = lax.dot_general(
            kT, ds, (((1,), (1,)), ((), ())), preferred_element_type=jnp.float32
        ).astype(dqkv_ref.dtype)
        dk_acc = dk_acc + jnp.dot(qT_b, ds, preferred_element_type=jnp.float32)
    dqkv_ref[1] = dk_acc.astype(dqkv_ref.dtype)
    dqkv_ref[2] = dv_acc.astype(dqkv_ref.dtype)


def fused_attention(qkvT, doT, keep_row, heads):
    _, c, n = qkvT.shape
    d = c // heads
    scale = d ** (-0.5)
    kernel = functools.partial(_attn_kernel, scale=scale, n=n, tq=TQ)
    flops = heads * 6 * 2 * n * n * d
    return pl.pallas_call(
        kernel,
        grid=(heads,),
        in_specs=[
            pl.BlockSpec((3, d, n), lambda h: (0, h, 0)),
            pl.BlockSpec((d, n), lambda h: (h, 0)),
            pl.BlockSpec((1, n), lambda h: (0, 0)),
        ],
        out_specs=[
            pl.BlockSpec((d, n), lambda h: (h, 0)),
            pl.BlockSpec((3, d, n), lambda h: (0, h, 0)),
        ],
        out_shape=[
            jax.ShapeDtypeStruct((c, n), jnp.bfloat16),
            jax.ShapeDtypeStruct((3, c, n), jnp.bfloat16),
        ],
        compiler_params=pltpu.CompilerParams(dimension_semantics=("arbitrary",)),
        cost_estimate=pl.CostEstimate(
            flops=flops, transcendentals=heads * n * n, bytes_accessed=2 * 8 * c * n
        ),
    )(qkvT, doT, keep_row)


def relayout_pair(first, second):
    size_x = lax.axis_size("gx")
    size_y = lax.axis_size("gy")
    first_s = first.reshape(size_x * size_y, -1, first.shape[1])
    second_s = second.reshape(size_x * size_y, -1)
    moved_a, moved_b = (
        lax.all_to_all(first_s, ("gx", "gy"), split_axis=0, concat_axis=0, tiled=True),
        lax.all_to_all(second_s, ("gx", "gy"), split_axis=0, concat_axis=0, tiled=True),
    )
    return (moved_a.reshape(first.shape), moved_b.reshape(second.shape))


def relayout_one(array):
    size_x = lax.axis_size("gx")
    size_y = lax.axis_size("gy")
    shaped = array.reshape(size_x * size_y, -1, array.shape[1])
    moved = lax.all_to_all(shaped, ("gx", "gy"), split_axis=0, concat_axis=0, tiled=True)
    return moved.reshape(array.shape)


def shards(features, valid, cotangent, gamma, w_qkv, w_out):
    rows, width = features.shape
    patches = rows // K
    nodes = rows * lax.axis_size("gx") * lax.axis_size("gy")
    inverse_root = float(nodes) ** (-0.5)
    input_rows, occupied = relayout_pair(features, valid.astype(jnp.bfloat16))
    normalized_input, reciprocal_deviation, hidden_state = layer_norm_apply(input_rows, gamma)
    qkvT = lax.dot_general(
        w_qkv, hidden_state, (((0,), (1,)), ((), ())), preferred_element_type=jnp.float32
    ).astype(jnp.bfloat16)
    y_keep = occupied.astype(jnp.float32).reshape(1, rows)
    gt = relayout_one(cotangent)
    d_attnT = lax.dot_general(
        w_out, gt, (((1,), (1,)), ((), ())), preferred_element_type=jnp.float32
    ).astype(jnp.bfloat16)
    attnT, d_qkvT = fused_attention(qkvT.reshape(3, width, rows), d_attnT, y_keep, HEADS)
    d_qkvT = d_qkvT.reshape(3 * width, rows)
    y_val = (
        input_rows.astype(jnp.float32)
        + lax.dot_general(attnT, w_out, (((0,), (0,)), ((), ())), preferred_element_type=jnp.float32)
    ).astype(jnp.bfloat16)
    y_plain = relayout_one(y_val)
    local_wout = jnp.dot(attnT, gt, preferred_element_type=jnp.float32)
    local_wqkv = lax.dot_general(
        hidden_state, d_qkvT, (((0,), (1,)), ((), ())), preferred_element_type=jnp.float32
    )
    hidden_gradient = lax.dot_general(
        d_qkvT, w_qkv, (((0,), (1,)), ((), ())), preferred_element_type=jnp.float32
    )
    shard_gamma = jnp.sum(hidden_gradient * normalized_input, 0)
    scaled_output = hidden_gradient * gamma
    norm_gradient = reciprocal_deviation * (
        scaled_output
        - jnp.mean(scaled_output, -1, keepdims=True)
        - normalized_input * jnp.mean(scaled_output * normalized_input, -1, keepdims=True)
    )
    d_x = (gt.astype(jnp.float32) + norm_gradient).astype(jnp.bfloat16)
    total_wqkv, total_wout, total_gamma = lax.psum(
        (local_wqkv, local_wout, shard_gamma), ("gx", "gy")
    )
    dx_plain = relayout_one(d_x)
    return (
        y_plain,
        dx_plain,
        total_wqkv * inverse_root,
        total_wout * inverse_root,
        total_gamma * inverse_root,
    )


def solution(mesh):
    placed = (P(("gx", "gy"), None), P(("gx", "gy")), P(("gx", "gy"), None), P(), P(), P())
    return jax.shard_map(
        shards,
        mesh=mesh,
        in_specs=placed,
        out_specs=(P(("gx", "gy"), None), P(("gx", "gy"), None), P(), P(), P()),
        check_vma=False,
    )
```

```python
import functools

import jax
import jax.numpy as jnp
from jax import lax
from jax.experimental import pallas as pl
from jax.experimental.pallas import tpu as pltpu
from jax.sharding import PartitionSpec as P

HEADS = 16
K = 1024
TQ = 256


def layer_norm_apply(input_rows, gamma):
    xf = input_rows.astype(jnp.float32)
    centered_input = xf - jnp.mean(xf, -1, keepdims=True)
    reciprocal_deviation = lax.rsqrt(
        jnp.mean(centered_input * centered_input, -1, keepdims=True) + 1e-05
    )
    normalized_input = centered_input * reciprocal_deviation
    return (normalized_input, reciprocal_deviation, (normalized_input * gamma).astype(jnp.bfloat16))


def _attn_kernel(qkv_ref, do_ref, keep_ref, o_ref, dqkv_ref, *, scale, n, tq):
    qT = qkv_ref[0]
    kT = qkv_ref[1]
    vT = qkv_ref[2]
    doT = do_ref[...]
    keep = keep_ref[...] > 0.5
    d = qT.shape[0]
    dk_acc = jnp.zeros((d, n), jnp.float32)
    dv_acc = jnp.zeros((d, n), jnp.float32)
    for b in range(n // tq):
        cols = slice(b * tq, (b + 1) * tq)
        qT_b = qT[:, cols]
        doT_b = doT[:, cols]
        q_b = qT_b.T
        do_b = doT_b.T
        s = jnp.dot(q_b, kT, preferred_element_type=jnp.float32) * scale
        s = jnp.where(keep, s, -1e30)
        m = jnp.max(s, -1, keepdims=True)
        e = jnp.exp(s - m)
        l = jnp.sum(e, -1, keepdims=True)
        p = e * (1.0 / l)
        pb = p.astype(jnp.bfloat16)
        o_ref[:, cols] = lax.dot_general(
            vT, pb, (((1,), (1,)), ((), ())), preferred_element_type=jnp.float32
        ).astype(o_ref.dtype)
        dv_acc = dv_acc + jnp.dot(doT_b, pb, preferred_element_type=jnp.float32)
        dp = jnp.dot(do_b, vT, preferred_element_type=jnp.float32)
        rs = jnp.sum(dp * p, -1, keepdims=True)
        ds = (p * (dp - rs) * scale).astype(jnp.bfloat16)
        dqkv_ref[0, :, cols] = lax.dot_general(
            kT, ds, (((1,), (1,)), ((), ())), preferred_element_type=jnp.float32
        ).astype(dqkv_ref.dtype)
        dk_acc = dk_acc + jnp.dot(qT_b, ds, preferred_element_type=jnp.float32)
    dqkv_ref[1] = dk_acc.astype(dqkv_ref.dtype)
    dqkv_ref[2] = dv_acc.astype(dqkv_ref.dtype)


def fused_attention(qkvT, doT, keep_row, heads):
    _, c, n = qkvT.shape
    d = c // heads
    scale = d ** (-0.5)
    kernel = functools.partial(_attn_kernel, scale=scale, n=n, tq=TQ)
    flops = heads * 6 * 2 * n * n * d
    return pl.pallas_call(
        kernel,
        grid=(heads,),
        in_specs=[
            pl.BlockSpec((3, d, n), lambda h: (0, h, 0)),
            pl.BlockSpec((d, n), lambda h: (h, 0)),
            pl.BlockSpec((1, n), lambda h: (0, 0)),
        ],
        out_specs=[
            pl.BlockSpec((d, n), lambda h: (h, 0)),
            pl.BlockSpec((3, d, n), lambda h: (0, h, 0)),
        ],
        out_shape=[
            jax.ShapeDtypeStruct((c, n), jnp.bfloat16),
            jax.ShapeDtypeStruct((3, c, n), jnp.bfloat16),
        ],
        compiler_params=pltpu.CompilerParams(dimension_semantics=("arbitrary",)),
        cost_estimate=pl.CostEstimate(
            flops=flops, transcendentals=heads * n * n, bytes_accessed=2 * 8 * c * n
        ),
    )(qkvT, doT, keep_row)


def to_all(array):
    size = lax.axis_size("gx") * lax.axis_size("gy")
    shaped = array.reshape(size, -1, array.shape[-1])
    moved = lax.all_to_all(shaped, ("gx", "gy"), split_axis=0, concat_axis=0, tiled=True)
    return moved.reshape(array.shape)


def sum_all(parts):
    size = lax.axis_size("gx") * lax.axis_size("gy")
    matrix, vector = parts
    rows, cols = matrix.shape
    per = rows // size
    side = jnp.zeros((size, per, 128), jnp.float32).at[:, :, 0].set(vector.reshape(size, per))
    payload = jnp.concatenate([matrix.reshape(size, per, cols), side], 2)
    moved = lax.all_to_all(payload, ("gx", "gy"), split_axis=0, concat_axis=0, tiled=True)
    mine = jnp.sum(moved, 0, keepdims=True)
    spread = jnp.broadcast_to(mine, payload.shape)
    total = lax.all_to_all(spread, ("gx", "gy"), split_axis=0, concat_axis=0, tiled=True)
    return total[:, :, :cols].reshape(rows, cols), total[:, :, cols].reshape(rows)


def shards(features, valid, cotangent, gamma, w_qkv, w_out):
    rows, width = features.shape
    nodes = rows * lax.axis_size("gx") * lax.axis_size("gy")
    inverse_root = float(nodes) ** (-0.5)
    flag = jnp.zeros((rows, 128), jnp.bfloat16).at[:, 0].set(valid.astype(jnp.bfloat16))
    moved = to_all(jnp.concatenate([features, cotangent, flag], 1))
    input_rows = moved[:, :width]
    gt = moved[:, width : 2 * width]
    occupied = moved[:, 2 * width]
    normalized_input, reciprocal_deviation, hidden_state = layer_norm_apply(input_rows, gamma)
    qkvT = lax.dot_general(
        w_qkv, hidden_state, (((0,), (1,)), ((), ())), preferred_element_type=jnp.float32
    ).astype(jnp.bfloat16)
    keep_row = occupied.astype(jnp.float32).reshape(1, rows)
    d_attnT = lax.dot_general(
        w_out, gt, (((1,), (1,)), ((), ())), preferred_element_type=jnp.float32
    ).astype(jnp.bfloat16)
    attnT, d_qkvT = fused_attention(qkvT.reshape(3, width, rows), d_attnT, keep_row, HEADS)
    d_qkvT = d_qkvT.reshape(3 * width, rows)
    y_val = (
        input_rows.astype(jnp.float32)
        + lax.dot_general(attnT, w_out, (((0,), (0,)), ((), ())), preferred_element_type=jnp.float32)
    ).astype(jnp.bfloat16)
    y_plain = to_all(y_val)
    local_wout = jnp.dot(attnT, gt, preferred_element_type=jnp.float32)
    local_wqkv = lax.dot_general(
        hidden_state, d_qkvT, (((0,), (1,)), ((), ())), preferred_element_type=jnp.float32
    )
    hidden_gradient = lax.dot_general(
        d_qkvT, w_qkv, (((0,), (1,)), ((), ())), preferred_element_type=jnp.float32
    )
    shard_gamma = jnp.sum(hidden_gradient * normalized_input, 0)
    scaled_output = hidden_gradient * gamma
    norm_gradient = reciprocal_deviation * (
        scaled_output
        - jnp.mean(scaled_output, -1, keepdims=True)
        - normalized_input * jnp.mean(scaled_output * normalized_input, -1, keepdims=True)
    )
    d_x = (gt.astype(jnp.float32) + norm_gradient).astype(jnp.bfloat16)
    total_w, total_gamma = sum_all(
        (jnp.concatenate([local_wqkv, local_wout], 1), shard_gamma)
    )
    dx_plain = to_all(d_x)
    return (
        y_plain,
        dx_plain,
        total_w[:, : 3 * width] * inverse_root,
        total_w[:, 3 * width :] * inverse_root,
        total_gamma * inverse_root,
    )


def solution(mesh):
    placed = (P(("gx", "gy"), None), P(("gx", "gy")), P(("gx", "gy"), None), P(), P(), P())
    return jax.shard_map(
        shards,
        mesh=mesh,
        in_specs=placed,
        out_specs=(P(("gx", "gy"), None), P(("gx", "gy"), None), P(), P(), P()),
        check_vma=False,
    )
```

```python
import functools

import jax
import jax.numpy as jnp
from jax import lax
from jax.experimental import pallas as pl
from jax.experimental.pallas import tpu as pltpu
from jax.sharding import PartitionSpec as P


HEADS = 16
TQ = 256


def layer_norm_apply(input_rows, gamma):
    xf = input_rows.astype(jnp.float32)
    centered_input = xf - jnp.mean(xf, -1, keepdims=True)
    reciprocal_deviation = lax.rsqrt(
        jnp.mean(centered_input * centered_input, -1, keepdims=True) + 1e-05
    )
    normalized_input = centered_input * reciprocal_deviation
    return (normalized_input, reciprocal_deviation, (normalized_input * gamma).astype(jnp.bfloat16))


def _attn_kernel(qkv_ref, do_ref, keep_ref, o_ref, dqkv_ref, *, scale, n, tq):
    qT = qkv_ref[0]
    kT = qkv_ref[1]
    vT = qkv_ref[2]
    doT = do_ref[...]
    keep = keep_ref[...] > 0.5
    d = qT.shape[0]
    dk_acc = jnp.zeros((d, n), jnp.float32)
    dv_acc = jnp.zeros((d, n), jnp.float32)
    for b in range(n // tq):
        cols = slice(b * tq, (b + 1) * tq)
        qT_b = qT[:, cols]
        doT_b = doT[:, cols]
        q_b = qT_b.T
        do_b = doT_b.T
        s = jnp.dot(q_b, kT, preferred_element_type=jnp.float32) * scale
        s = jnp.where(keep, s, -1e30)
        m = jnp.max(s, -1, keepdims=True)
        e = jnp.exp(s - m)
        l = jnp.sum(e, -1, keepdims=True)
        p = e * (1.0 / l)
        pb = p.astype(jnp.bfloat16)
        o_ref[:, cols] = lax.dot_general(
            vT, pb, (((1,), (1,)), ((), ())), preferred_element_type=jnp.float32
        ).astype(o_ref.dtype)
        dv_acc = dv_acc + jnp.dot(doT_b, pb, preferred_element_type=jnp.float32)
        dp = jnp.dot(do_b, vT, preferred_element_type=jnp.float32)
        rs = jnp.sum(dp * p, -1, keepdims=True)
        ds = (p * (dp - rs) * scale).astype(jnp.bfloat16)
        dqkv_ref[0, :, cols] = lax.dot_general(
            kT, ds, (((1,), (1,)), ((), ())), preferred_element_type=jnp.float32
        ).astype(dqkv_ref.dtype)
        dk_acc = dk_acc + jnp.dot(qT_b, ds, preferred_element_type=jnp.float32)
    dqkv_ref[1] = dk_acc.astype(dqkv_ref.dtype)
    dqkv_ref[2] = dv_acc.astype(dqkv_ref.dtype)


def fused_attention(qkvT, doT, keep_row, heads, first, count):
    _, c, n = qkvT.shape
    d = c // heads
    scale = d ** (-0.5)
    kernel = functools.partial(_attn_kernel, scale=scale, n=n, tq=TQ)
    flops = count * 6 * 2 * n * n * d
    return pl.pallas_call(
        kernel,
        grid=(count,),
        in_specs=[
            pl.BlockSpec((3, d, n), lambda h: (0, h + first, 0)),
            pl.BlockSpec((d, n), lambda h: (h + first, 0)),
            pl.BlockSpec((1, n), lambda h: (0, 0)),
        ],
        out_specs=[
            pl.BlockSpec((d, n), lambda h: (h, 0)),
            pl.BlockSpec((3, d, n), lambda h: (0, h, 0)),
        ],
        out_shape=[
            jax.ShapeDtypeStruct((count * d, n), jnp.bfloat16),
            jax.ShapeDtypeStruct((3, count * d, n), jnp.bfloat16),
        ],
        compiler_params=pltpu.CompilerParams(dimension_semantics=("arbitrary",)),
        cost_estimate=pl.CostEstimate(
            flops=flops, transcendentals=count * n * n, bytes_accessed=2 * 8 * count * d * n
        ),
    )(qkvT, doT, keep_row)


def to_all(array):
    size = lax.axis_size("gx") * lax.axis_size("gy")
    shaped = array.reshape(size, -1, array.shape[-1])
    moved = lax.all_to_all(shaped, ("gx", "gy"), split_axis=0, concat_axis=0, tiled=True)
    return moved.reshape(array.shape)


def scatter_sum(payload):
    moved = lax.all_to_all(payload, ("gx", "gy"), split_axis=0, concat_axis=0, tiled=True)
    return jnp.sum(moved, 0, keepdims=True)


def gather_all(chunk, size):
    spread = jnp.broadcast_to(chunk, (size,) + chunk.shape[1:])
    return lax.all_to_all(spread, ("gx", "gy"), split_axis=0, concat_axis=0, tiled=True)


def half_grads(hidden_state, d_qkvT_half, attnT_half, gt):
    wq = lax.dot_general(
        hidden_state, d_qkvT_half.reshape(-1, d_qkvT_half.shape[-1]),
        (((0,), (1,)), ((), ())), preferred_element_type=jnp.float32,
    )
    wo = jnp.dot(attnT_half, gt, preferred_element_type=jnp.float32)
    return wq, wo


def block(features, valid, cotangent, gamma, w_qkv, w_out):
    rows, width = features.shape
    size = lax.axis_size("gx") * lax.axis_size("gy")
    nodes = rows * size
    inverse_root = float(nodes) ** (-0.5)
    half = HEADS // 2
    hw = width // 2
    flag = jnp.zeros((rows, 128), jnp.bfloat16).at[:, 0].set(valid.astype(jnp.bfloat16))
    moved = to_all(jnp.concatenate([features, cotangent, flag], 1))
    input_rows = moved[:, :width]
    gt = moved[:, width : 2 * width]
    occupied = moved[:, 2 * width]
    normalized_input, reciprocal_deviation, hidden_state = layer_norm_apply(input_rows, gamma)
    qkvT = lax.dot_general(
        w_qkv, hidden_state, (((0,), (1,)), ((), ())), preferred_element_type=jnp.float32
    ).astype(jnp.bfloat16).reshape(3, width, rows)
    keep_row = occupied.astype(jnp.float32).reshape(1, rows)
    d_attnT = lax.dot_general(
        w_out, gt, (((1,), (1,)), ((), ())), preferred_element_type=jnp.float32
    ).astype(jnp.bfloat16)

    attn_a, dqkv_a = fused_attention(qkvT, d_attnT, keep_row, HEADS, 0, half)
    wq_a, wo_a = half_grads(hidden_state, dqkv_a, attn_a, gt)
    sizes_a = (wq_a.size, wo_a.size)
    pay_a = jnp.concatenate([wq_a.reshape(-1), wo_a.reshape(-1)]).reshape(size, -1, 128)
    mine_a = scatter_sum(pay_a)
    attn_b, dqkv_b = fused_attention(qkvT, d_attnT, keep_row, HEADS, half, half)
    total_a = gather_all(mine_a, size).reshape(-1)

    attnT = jnp.concatenate([attn_a, attn_b], 0)
    y_val = (
        input_rows.astype(jnp.float32)
        + lax.dot_general(attnT, w_out, (((0,), (0,)), ((), ())), preferred_element_type=jnp.float32)
    ).astype(jnp.bfloat16)
    y_plain = to_all(y_val)
    wq_b, wo_b = half_grads(hidden_state, dqkv_b, attn_b, gt)
    d_qkvT = jnp.concatenate([dqkv_a, dqkv_b], 1).reshape(3 * width, rows)
    hidden_gradient = lax.dot_general(
        d_qkvT, w_qkv, (((0,), (1,)), ((), ())), preferred_element_type=jnp.float32
    )
    shard_gamma = jnp.sum(hidden_gradient * normalized_input, 0)
    scaled_output = hidden_gradient * gamma
    norm_gradient = reciprocal_deviation * (
        scaled_output
        - jnp.mean(scaled_output, -1, keepdims=True)
        - normalized_input * jnp.mean(scaled_output * normalized_input, -1, keepdims=True)
    )
    d_x = (gt.astype(jnp.float32) + norm_gradient).astype(jnp.bfloat16)
    main_b = jnp.concatenate([wq_b.reshape(-1), wo_b.reshape(-1)]).reshape(size, -1, 128)
    per = width // size
    side = jnp.zeros((size, 1, 128), jnp.float32).at[:, 0, :per].set(shard_gamma.reshape(size, per))
    pay_b = jnp.concatenate([main_b, side], 1)
    mine_b = scatter_sum(pay_b)
    dx_plain = to_all(d_x)
    total_b = gather_all(mine_b, size)
    gamma_total = total_b[:, -1, :per].reshape(width)
    flat_b = total_b[:, :-1, :].reshape(-1)

    def unpack(flat):
        wq = flat[: sizes_a[0]].reshape(width, 3, hw)
        wo = flat[sizes_a[0] :].reshape(hw, width)
        return wq, wo

    wq_ta, wo_ta = unpack(total_a)
    wq_tb, wo_tb = unpack(flat_b)
    total_wqkv = jnp.concatenate([wq_ta, wq_tb], 2).reshape(width, 3 * width)
    total_wout = jnp.concatenate([wo_ta, wo_tb], 0)
    return (
        y_plain,
        dx_plain,
        total_wqkv * inverse_root,
        total_wout * inverse_root,
        gamma_total * inverse_root,
    )


def solution(mesh):
    placed = (P(("gx", "gy"), None), P(("gx", "gy")), P(("gx", "gy"), None), P(), P(), P())
    return jax.shard_map(
        block,
        mesh=mesh,
        in_specs=placed,
        out_specs=(P(("gx", "gy"), None), P(("gx", "gy"), None), P(), P(), P()),
        check_vma=False,
    )
```

```python
import functools

import jax
import jax.numpy as jnp
from jax import lax
from jax.experimental import pallas as pl
from jax.experimental.pallas import tpu as pltpu
from jax.sharding import PartitionSpec as P


HEADS = 16
TQ = 256


def layer_norm_apply(input_rows, gamma):
    xf = input_rows.astype(jnp.float32)
    centered_input = xf - jnp.mean(xf, -1, keepdims=True)
    reciprocal_deviation = lax.rsqrt(
        jnp.mean(centered_input * centered_input, -1, keepdims=True) + 1e-05
    )
    normalized_input = centered_input * reciprocal_deviation
    return (normalized_input, reciprocal_deviation, (normalized_input * gamma).astype(jnp.bfloat16))


def _attn_kernel(qkv_ref, do_ref, keep_ref, o_ref, dqkv_ref, *, scale, n, tq):
    qT = qkv_ref[0]
    kT = qkv_ref[1]
    vT = qkv_ref[2]
    doT = do_ref[...]
    keep = keep_ref[...] > 0.5
    d = qT.shape[0]
    dk_acc = jnp.zeros((d, n), jnp.float32)
    dv_acc = jnp.zeros((d, n), jnp.float32)
    for b in range(n // tq):
        cols = slice(b * tq, (b + 1) * tq)
        qT_b = qT[:, cols]
        doT_b = doT[:, cols]
        q_b = qT_b.T
        do_b = doT_b.T
        s = jnp.dot(q_b, kT, preferred_element_type=jnp.float32) * scale
        s = jnp.where(keep, s, -1e30)
        m = jnp.max(s, -1, keepdims=True)
        e = jnp.exp(s - m)
        l = jnp.sum(e, -1, keepdims=True)
        p = e * (1.0 / l)
        pb = p.astype(jnp.bfloat16)
        o_ref[:, cols] = lax.dot_general(
            vT, pb, (((1,), (1,)), ((), ())), preferred_element_type=jnp.float32
        ).astype(o_ref.dtype)
        dv_acc = dv_acc + jnp.dot(doT_b, pb, preferred_element_type=jnp.float32)
        dp = jnp.dot(do_b, vT, preferred_element_type=jnp.float32)
        rs = jnp.sum(dp * p, -1, keepdims=True)
        ds = (p * (dp - rs) * scale).astype(jnp.bfloat16)
        dqkv_ref[0, :, cols] = lax.dot_general(
            kT, ds, (((1,), (1,)), ((), ())), preferred_element_type=jnp.float32
        ).astype(dqkv_ref.dtype)
        dk_acc = dk_acc + jnp.dot(qT_b, ds, preferred_element_type=jnp.float32)
    dqkv_ref[1] = dk_acc.astype(dqkv_ref.dtype)
    dqkv_ref[2] = dv_acc.astype(dqkv_ref.dtype)


def fused_attention(qkvT, doT, keep_row, heads, first, count):
    _, c, n = qkvT.shape
    d = c // heads
    scale = d ** (-0.5)
    kernel = functools.partial(_attn_kernel, scale=scale, n=n, tq=TQ)
    flops = count * 6 * 2 * n * n * d
    return pl.pallas_call(
        kernel,
        grid=(count,),
        in_specs=[
            pl.BlockSpec((3, d, n), lambda h: (0, h + first, 0)),
            pl.BlockSpec((d, n), lambda h: (h + first, 0)),
            pl.BlockSpec((1, n), lambda h: (0, 0)),
        ],
        out_specs=[
            pl.BlockSpec((d, n), lambda h: (h, 0)),
            pl.BlockSpec((3, d, n), lambda h: (0, h, 0)),
        ],
        out_shape=[
            jax.ShapeDtypeStruct((count * d, n), jnp.bfloat16),
            jax.ShapeDtypeStruct((3, count * d, n), jnp.bfloat16),
        ],
        compiler_params=pltpu.CompilerParams(dimension_semantics=("arbitrary",)),
        cost_estimate=pl.CostEstimate(
            flops=flops, transcendentals=count * n * n, bytes_accessed=2 * 8 * count * d * n
        ),
    )(qkvT, doT, keep_row)


def to_all(array):
    size = lax.axis_size("gx") * lax.axis_size("gy")
    shaped = array.reshape(size, -1, array.shape[-1])
    moved = lax.all_to_all(shaped, ("gx", "gy"), split_axis=0, concat_axis=0, tiled=True)
    return moved.reshape(array.shape)


def scatter_sum(payload):
    moved = lax.all_to_all(payload, ("gx", "gy"), split_axis=0, concat_axis=0, tiled=True)
    return jnp.sum(moved, 0, keepdims=True)


def gather_all(chunk, size):
    spread = jnp.broadcast_to(chunk, (size,) + chunk.shape[1:])
    return lax.all_to_all(spread, ("gx", "gy"), split_axis=0, concat_axis=0, tiled=True)


def half_grads(hidden_state, d_qkvT_half, attnT_half, gt):
    wq = lax.dot_general(
        hidden_state, d_qkvT_half.reshape(-1, d_qkvT_half.shape[-1]),
        (((0,), (1,)), ((), ())), preferred_element_type=jnp.float32,
    )
    wo = jnp.dot(attnT_half, gt, preferred_element_type=jnp.float32)
    return wq, wo


def block(features, valid, cotangent, gamma, w_qkv, w_out):
    rows, width = features.shape
    size = lax.axis_size("gx") * lax.axis_size("gy")
    nodes = rows * size
    inverse_root = float(nodes) ** (-0.5)
    half = HEADS // 2
    hw = width // 2
    flag = jnp.zeros((rows, 128), jnp.bfloat16).at[:, 0].set(valid.astype(jnp.bfloat16))
    moved = to_all(jnp.concatenate([features, cotangent, flag], 1))
    input_rows = moved[:, :width]
    gt = moved[:, width : 2 * width]
    occupied = moved[:, 2 * width]
    normalized_input, reciprocal_deviation, hidden_state = layer_norm_apply(input_rows, gamma)
    qkvT = lax.dot_general(
        w_qkv, hidden_state, (((0,), (1,)), ((), ())), preferred_element_type=jnp.float32
    ).astype(jnp.bfloat16).reshape(3, width, rows)
    keep_row = occupied.astype(jnp.float32).reshape(1, rows)
    d_attnT = lax.dot_general(
        w_out, gt, (((1,), (1,)), ((), ())), preferred_element_type=jnp.float32
    ).astype(jnp.bfloat16)

    attn_a, dqkv_a = fused_attention(qkvT, d_attnT, keep_row, HEADS, 0, half)
    wq_a, wo_a = half_grads(hidden_state, dqkv_a, attn_a, gt)
    sizes_a = (wq_a.size, wo_a.size)
    pay_a = jnp.concatenate([wq_a.reshape(-1), wo_a.reshape(-1)]).reshape(size, -1, 128)
    mine_a = scatter_sum(pay_a)
    attn_b, dqkv_b = fused_attention(qkvT, d_attnT, keep_row, HEADS, half, half)
    total_a = gather_all(mine_a, size).reshape(-1)

    attnT = jnp.concatenate([attn_a, attn_b], 0)
    y_val = (
        input_rows.astype(jnp.float32)
        + lax.dot_general(
            attnT, w_out, (((0,), (0,)), ((), ())), preferred_element_type=jnp.float32
        )
    ).astype(jnp.bfloat16)
    wq_b, wo_b = half_grads(hidden_state, dqkv_b, attn_b, gt)
    d_qkvT = jnp.concatenate([dqkv_a, dqkv_b], 1).reshape(3 * width, rows)
    hidden_gradient = lax.dot_general(
        d_qkvT, w_qkv, (((0,), (1,)), ((), ())), preferred_element_type=jnp.float32
    )
    shard_gamma = jnp.sum(hidden_gradient * normalized_input, 0)
    scaled_output = hidden_gradient * gamma
    norm_gradient = reciprocal_deviation * (
        scaled_output
        - jnp.mean(scaled_output, -1, keepdims=True)
        - normalized_input * jnp.mean(scaled_output * normalized_input, -1, keepdims=True)
    )
    d_x = (gt.astype(jnp.float32) + norm_gradient).astype(jnp.bfloat16)
    main_b = jnp.concatenate([wq_b.reshape(-1), wo_b.reshape(-1)]).reshape(size, -1, 128)
    per = width // size
    side = jnp.zeros((size, 1, 128), jnp.float32).at[:, 0, :per].set(shard_gamma.reshape(size, per))
    pay_b = jnp.concatenate([main_b, side], 1)
    lead = pay_b.astype(jnp.bfloat16)
    rest = (pay_b - lead.astype(jnp.float32)).astype(jnp.bfloat16)
    nb = pay_b.shape[1]
    coded = jnp.concatenate([lead, rest], 1).reshape(size, nb, 2 * 128)
    per_dev = rows // size
    payload = jnp.concatenate(
        [d_x.reshape(size, per_dev, width), y_val.reshape(size, per_dev, width), coded], 1
    )
    moved_b = lax.all_to_all(payload, ("gx", "gy"), split_axis=0, concat_axis=0, tiled=True)
    dx_plain = moved_b[:, :per_dev].reshape(rows, width)
    y_plain = moved_b[:, per_dev : 2 * per_dev].reshape(rows, width)
    got = moved_b[:, 2 * per_dev :].reshape(size, 2 * nb, 128).astype(jnp.float32)
    mine_b = jnp.sum(got[:, :nb] + got[:, nb:], 0, keepdims=True)
    total_b = gather_all(mine_b, size)
    gamma_total = total_b[:, -1, :per].reshape(width)
    flat_b = total_b[:, :-1, :].reshape(-1)

    def unpack(flat):
        wq = flat[: sizes_a[0]].reshape(width, 3, hw)
        wo = flat[sizes_a[0] :].reshape(hw, width)
        return wq, wo

    wq_ta, wo_ta = unpack(total_a)
    wq_tb, wo_tb = unpack(flat_b)
    total_wqkv = jnp.concatenate([wq_ta, wq_tb], 2).reshape(width, 3 * width)
    total_wout = jnp.concatenate([wo_ta, wo_tb], 0)
    return (
        y_plain,
        dx_plain,
        total_wqkv * inverse_root,
        total_wout * inverse_root,
        gamma_total * inverse_root,
    )


def solution(mesh):
    placed = (P(("gx", "gy"), None), P(("gx", "gy")), P(("gx", "gy"), None), P(), P(), P())
    return jax.shard_map(
        block,
        mesh=mesh,
        in_specs=placed,
        out_specs=(P(("gx", "gy"), None), P(("gx", "gy"), None), P(), P(), P()),
        check_vma=False,
    )
```

```python
import functools

import jax
import jax.numpy as jnp
from jax import lax
from jax.experimental import pallas as pl
from jax.experimental.pallas import tpu as pltpu
from jax.sharding import PartitionSpec as P

HEADS = 16
K = 1024
TQ = 256


def layer_norm_apply(input_rows, gamma):
    xf = input_rows.astype(jnp.float32)
    centered_input = xf - jnp.mean(xf, -1, keepdims=True)
    reciprocal_deviation = lax.rsqrt(
        jnp.mean(centered_input * centered_input, -1, keepdims=True) + 1e-05
    )
    normalized_input = centered_input * reciprocal_deviation
    return (normalized_input, reciprocal_deviation, (normalized_input * gamma).astype(jnp.bfloat16))


def _attn_kernel(qkv_ref, do_ref, keep_ref, o_ref, dqkv_ref, *, scale, n, tq):
    qT = qkv_ref[0]
    kT = qkv_ref[1]
    vT = qkv_ref[2]
    doT = do_ref[...]
    keep = keep_ref[...] > 0.5
    d = qT.shape[0]
    dk_acc = jnp.zeros((d, n), jnp.float32)
    dv_acc = jnp.zeros((d, n), jnp.float32)
    for b in range(n // tq):
        cols = slice(b * tq, (b + 1) * tq)
        qT_b = qT[:, cols]
        doT_b = doT[:, cols]
        q_b = qT_b.T
        do_b = doT_b.T
        s = jnp.dot(q_b, kT, preferred_element_type=jnp.float32) * scale
        s = jnp.where(keep, s, -1e30)
        m = jnp.max(s, -1, keepdims=True)
        e = jnp.exp(s - m)
        l = jnp.sum(e, -1, keepdims=True)
        p = e * (1.0 / l)
        pb = p.astype(jnp.bfloat16)
        o_ref[:, cols] = lax.dot_general(
            vT, pb, (((1,), (1,)), ((), ())), preferred_element_type=jnp.float32
        ).astype(o_ref.dtype)
        dv_acc = dv_acc + jnp.dot(doT_b, pb, preferred_element_type=jnp.float32)
        dp = jnp.dot(do_b, vT, preferred_element_type=jnp.float32)
        rs = jnp.sum(dp * p, -1, keepdims=True)
        ds = (p * (dp - rs) * scale).astype(jnp.bfloat16)
        dqkv_ref[0, :, cols] = lax.dot_general(
            kT, ds, (((1,), (1,)), ((), ())), preferred_element_type=jnp.float32
        ).astype(dqkv_ref.dtype)
        dk_acc = dk_acc + jnp.dot(qT_b, ds, preferred_element_type=jnp.float32)
    dqkv_ref[1] = dk_acc.astype(dqkv_ref.dtype)
    dqkv_ref[2] = dv_acc.astype(dqkv_ref.dtype)


def fused_attention(qkvT, doT, keep_row, heads):
    _, c, n = qkvT.shape
    d = c // heads
    scale = d ** (-0.5)
    kernel = functools.partial(_attn_kernel, scale=scale, n=n, tq=TQ)
    flops = heads * 6 * 2 * n * n * d
    return pl.pallas_call(
        kernel,
        grid=(heads,),
        in_specs=[
            pl.BlockSpec((3, d, n), lambda h: (0, h, 0)),
            pl.BlockSpec((d, n), lambda h: (h, 0)),
            pl.BlockSpec((1, n), lambda h: (0, 0)),
        ],
        out_specs=[
            pl.BlockSpec((d, n), lambda h: (h, 0)),
            pl.BlockSpec((3, d, n), lambda h: (0, h, 0)),
        ],
        out_shape=[
            jax.ShapeDtypeStruct((c, n), jnp.bfloat16),
            jax.ShapeDtypeStruct((3, c, n), jnp.bfloat16),
        ],
        compiler_params=pltpu.CompilerParams(dimension_semantics=("arbitrary",)),
        cost_estimate=pl.CostEstimate(
            flops=flops, transcendentals=heads * n * n, bytes_accessed=2 * 8 * c * n
        ),
    )(qkvT, doT, keep_row)


def to_all(array):
    size = lax.axis_size("gx") * lax.axis_size("gy")
    shaped = array.reshape(size, -1, array.shape[-1])
    moved = lax.all_to_all(shaped, ("gx", "gy"), split_axis=0, concat_axis=0, tiled=True)
    return moved.reshape(array.shape)


def sum_all(parts):
    size = lax.axis_size("gx") * lax.axis_size("gy")
    matrix, vector = parts
    rows, cols = matrix.shape
    per = rows // size
    side = jnp.zeros((size, per, 128), jnp.float32).at[:, :, 0].set(vector.reshape(size, per))
    payload = jnp.concatenate([matrix.reshape(size, per, cols), side], 2)
    moved = lax.all_to_all(
        payload.astype(jnp.bfloat16), ("gx", "gy"), split_axis=0, concat_axis=0, tiled=True
    )
    mine = jnp.sum(moved.astype(jnp.float32), 0, keepdims=True)
    spread = jnp.broadcast_to(mine.astype(jnp.bfloat16), payload.shape)
    total = lax.all_to_all(
        spread, ("gx", "gy"), split_axis=0, concat_axis=0, tiled=True
    ).astype(jnp.float32)
    return total[:, :, :cols].reshape(rows, cols), total[:, :, cols].reshape(rows)


def shards(features, valid, cotangent, gamma, w_qkv, w_out):
    rows, width = features.shape
    nodes = rows * lax.axis_size("gx") * lax.axis_size("gy")
    inverse_root = float(nodes) ** (-0.5)
    flag = jnp.zeros((rows, 128), jnp.bfloat16).at[:, 0].set(valid.astype(jnp.bfloat16))
    moved = to_all(jnp.concatenate([features, cotangent, flag], 1))
    input_rows = moved[:, :width]
    gt = moved[:, width : 2 * width]
    occupied = moved[:, 2 * width]
    normalized_input, reciprocal_deviation, hidden_state = layer_norm_apply(input_rows, gamma)
    qkvT = lax.dot_general(
        w_qkv, hidden_state, (((0,), (1,)), ((), ())), preferred_element_type=jnp.float32
    ).astype(jnp.bfloat16)
    keep_row = occupied.astype(jnp.float32).reshape(1, rows)
    d_attnT = lax.dot_general(
        w_out, gt, (((1,), (1,)), ((), ())), preferred_element_type=jnp.float32
    ).astype(jnp.bfloat16)
    attnT, d_qkvT = fused_attention(qkvT.reshape(3, width, rows), d_attnT, keep_row, HEADS)
    d_qkvT = d_qkvT.reshape(3 * width, rows)
    y_val = (
        input_rows.astype(jnp.float32)
        + lax.dot_general(attnT, w_out, (((0,), (0,)), ((), ())), preferred_element_type=jnp.float32)
    ).astype(jnp.bfloat16)
    y_plain = to_all(y_val)
    local_wout = jnp.dot(attnT, gt, preferred_element_type=jnp.float32)
    local_wqkv = lax.dot_general(
        hidden_state, d_qkvT, (((0,), (1,)), ((), ())), preferred_element_type=jnp.float32
    )
    hidden_gradient = lax.dot_general(
        d_qkvT, w_qkv, (((0,), (1,)), ((), ())), preferred_element_type=jnp.float32
    )
    shard_gamma = jnp.sum(hidden_gradient * normalized_input, 0)
    scaled_output = hidden_gradient * gamma
    norm_gradient = reciprocal_deviation * (
        scaled_output
        - jnp.mean(scaled_output, -1, keepdims=True)
        - normalized_input * jnp.mean(scaled_output * normalized_input, -1, keepdims=True)
    )
    d_x = (gt.astype(jnp.float32) + norm_gradient).astype(jnp.bfloat16)
    total_w, total_gamma = sum_all(
        (jnp.concatenate([local_wqkv, local_wout], 1), shard_gamma)
    )
    dx_plain = to_all(d_x)
    return (
        y_plain,
        dx_plain,
        total_w[:, : 3 * width] * inverse_root,
        total_w[:, 3 * width :] * inverse_root,
        total_gamma * inverse_root,
    )


def solution(mesh):
    placed = (P(("gx", "gy"), None), P(("gx", "gy")), P(("gx", "gy"), None), P(), P(), P())
    return jax.shard_map(
        shards,
        mesh=mesh,
        in_specs=placed,
        out_specs=(P(("gx", "gy"), None), P(("gx", "gy"), None), P(), P(), P()),
        check_vma=False,
    )
```

```python
import functools

import jax
import jax.numpy as jnp
from jax import lax
from jax.experimental import pallas as pl
from jax.experimental.pallas import tpu as pltpu
from jax.sharding import PartitionSpec as P

HEADS = 16
K = 1024
TQ = 512


def layer_norm_apply(input_rows, gamma):
    xf = input_rows.astype(jnp.float32)
    centered_input = xf - jnp.mean(xf, -1, keepdims=True)
    reciprocal_deviation = lax.rsqrt(
        jnp.mean(centered_input * centered_input, -1, keepdims=True) + 1e-05
    )
    normalized_input = centered_input * reciprocal_deviation
    return (normalized_input, reciprocal_deviation, (normalized_input * gamma).astype(jnp.bfloat16))


def _attn_kernel(qkv_ref, do_ref, keep_ref, o_ref, dqkv_ref, *, scale, n, tq):
    qT = qkv_ref[0]
    kT = qkv_ref[1]
    vT = qkv_ref[2]
    doT = do_ref[...]
    keep = keep_ref[...] > 0.5
    d = qT.shape[0]
    dk_acc = jnp.zeros((d, n), jnp.float32)
    dv_acc = jnp.zeros((d, n), jnp.float32)
    k_rows = kT.T
    v_rows = vT.T
    for b in range(n // tq):
        cols = slice(b * tq, (b + 1) * tq)
        qT_b = qT[:, cols]
        doT_b = doT[:, cols]
        q_b = qT_b.T
        do_b = doT_b.T
        s = jnp.dot(q_b, kT, preferred_element_type=jnp.float32) * scale
        s = jnp.where(keep, s, -1e30)
        m = jnp.max(s, -1, keepdims=True)
        e = jnp.exp(s - m)
        l = jnp.sum(e, -1, keepdims=True)
        p = e * (1.0 / l)
        pb = p.astype(jnp.bfloat16)
        o_ref[:, cols] = (
            jnp.dot(pb, v_rows, preferred_element_type=jnp.float32).T.astype(o_ref.dtype)
        )
        dv_acc = dv_acc + jnp.dot(doT_b, pb, preferred_element_type=jnp.float32)
        dp = jnp.dot(do_b, vT, preferred_element_type=jnp.float32)
        rs = jnp.sum(dp * p, -1, keepdims=True)
        ds = (p * (dp - rs) * scale).astype(jnp.bfloat16)
        dqkv_ref[0, :, cols] = (
            jnp.dot(ds, k_rows, preferred_element_type=jnp.float32).T.astype(dqkv_ref.dtype)
        )
        dk_acc = dk_acc + jnp.dot(qT_b, ds, preferred_element_type=jnp.float32)
    dqkv_ref[1] = dk_acc.astype(dqkv_ref.dtype)
    dqkv_ref[2] = dv_acc.astype(dqkv_ref.dtype)


def fused_attention(qkvT, doT, keep_row, heads):
    _, c, n = qkvT.shape
    d = c // heads
    scale = d ** (-0.5)
    kernel = functools.partial(_attn_kernel, scale=scale, n=n, tq=TQ)
    flops = heads * 6 * 2 * n * n * d
    return pl.pallas_call(
        kernel,
        grid=(heads,),
        in_specs=[
            pl.BlockSpec((3, d, n), lambda h: (0, h, 0)),
            pl.BlockSpec((d, n), lambda h: (h, 0)),
            pl.BlockSpec((1, n), lambda h: (0, 0)),
        ],
        out_specs=[
            pl.BlockSpec((d, n), lambda h: (h, 0)),
            pl.BlockSpec((3, d, n), lambda h: (0, h, 0)),
        ],
        out_shape=[
            jax.ShapeDtypeStruct((c, n), jnp.bfloat16),
            jax.ShapeDtypeStruct((3, c, n), jnp.bfloat16),
        ],
        compiler_params=pltpu.CompilerParams(dimension_semantics=("arbitrary",)),
        cost_estimate=pl.CostEstimate(
            flops=flops, transcendentals=heads * n * n, bytes_accessed=2 * 8 * c * n
        ),
    )(qkvT, doT, keep_row)


def to_all(array):
    size = lax.axis_size("gx") * lax.axis_size("gy")
    shaped = array.reshape(size, -1, array.shape[-1])
    moved = lax.all_to_all(shaped, ("gx", "gy"), split_axis=0, concat_axis=0, tiled=True)
    return moved.reshape(array.shape)


def sum_all(parts):
    size = lax.axis_size("gx") * lax.axis_size("gy")
    matrix, vector = parts
    rows, cols = matrix.shape
    per = rows // size
    side = jnp.zeros((size, per, 128), jnp.float32).at[:, :, 0].set(vector.reshape(size, per))
    payload = jnp.concatenate([matrix.reshape(size, per, cols), side], 2)
    moved = lax.all_to_all(
        payload.astype(jnp.bfloat16), ("gx", "gy"), split_axis=0, concat_axis=0, tiled=True
    )
    mine = jnp.sum(moved.astype(jnp.float32), 0, keepdims=True)
    spread = jnp.broadcast_to(mine.astype(jnp.bfloat16), payload.shape)
    total = lax.all_to_all(
        spread, ("gx", "gy"), split_axis=0, concat_axis=0, tiled=True
    ).astype(jnp.float32)
    return total[:, :, :cols].reshape(rows, cols), total[:, :, cols].reshape(rows)


def shards(features, valid, cotangent, gamma, w_qkv, w_out):
    rows, width = features.shape
    nodes = rows * lax.axis_size("gx") * lax.axis_size("gy")
    inverse_root = float(nodes) ** (-0.5)
    flag = jnp.zeros((rows, 128), jnp.bfloat16).at[:, 0].set(valid.astype(jnp.bfloat16))
    moved = to_all(jnp.concatenate([features, cotangent, flag], 1))
    input_rows = moved[:, :width]
    gt = moved[:, width : 2 * width]
    occupied = moved[:, 2 * width]
    normalized_input, reciprocal_deviation, hidden_state = layer_norm_apply(input_rows, gamma)
    qkvT = lax.dot_general(
        w_qkv, hidden_state, (((0,), (1,)), ((), ())), preferred_element_type=jnp.float32
    ).astype(jnp.bfloat16)
    keep_row = occupied.astype(jnp.float32).reshape(1, rows)
    d_attnT = lax.dot_general(
        w_out, gt, (((1,), (1,)), ((), ())), preferred_element_type=jnp.float32
    ).astype(jnp.bfloat16)
    attnT, d_qkvT = fused_attention(qkvT.reshape(3, width, rows), d_attnT, keep_row, HEADS)
    d_qkvT = d_qkvT.reshape(3 * width, rows)
    y_val = (
        input_rows.astype(jnp.float32)
        + lax.dot_general(attnT, w_out, (((0,), (0,)), ((), ())), preferred_element_type=jnp.float32)
    ).astype(jnp.bfloat16)
    y_plain = to_all(y_val)
    local_wout = jnp.dot(attnT, gt, preferred_element_type=jnp.float32)
    local_wqkv = lax.dot_general(
        hidden_state, d_qkvT, (((0,), (1,)), ((), ())), preferred_element_type=jnp.float32
    )
    hidden_gradient = lax.dot_general(
        d_qkvT, w_qkv, (((0,), (1,)), ((), ())), preferred_element_type=jnp.float32
    )
    shard_gamma = jnp.sum(hidden_gradient * normalized_input, 0)
    scaled_output = hidden_gradient * gamma
    norm_gradient = reciprocal_deviation * (
        scaled_output
        - jnp.mean(scaled_output, -1, keepdims=True)
        - normalized_input * jnp.mean(scaled_output * normalized_input, -1, keepdims=True)
    )
    d_x = (gt.astype(jnp.float32) + norm_gradient).astype(jnp.bfloat16)
    total_w, total_gamma = sum_all(
        (jnp.concatenate([local_wqkv, local_wout], 1), shard_gamma)
    )
    dx_plain = to_all(d_x)
    return (
        y_plain,
        dx_plain,
        total_w[:, : 3 * width] * inverse_root,
        total_w[:, 3 * width :] * inverse_root,
        total_gamma * inverse_root,
    )


def solution(mesh):
    placed = (P(("gx", "gy"), None), P(("gx", "gy")), P(("gx", "gy"), None), P(), P(), P())
    return jax.shard_map(
        shards,
        mesh=mesh,
        in_specs=placed,
        out_specs=(P(("gx", "gy"), None), P(("gx", "gy"), None), P(), P(), P()),
        check_vma=False,
    )
```

```python
import functools

import jax
import jax.numpy as jnp
from jax import lax
from jax.experimental import pallas as pl
from jax.experimental.pallas import tpu as pltpu
from jax.sharding import PartitionSpec as P


HEADS = 16
TQ = 512


def layer_norm_apply(input_rows, gamma):
    xf = input_rows.astype(jnp.float32)
    centered_input = xf - jnp.mean(xf, -1, keepdims=True)
    reciprocal_deviation = lax.rsqrt(
        jnp.mean(centered_input * centered_input, -1, keepdims=True) + 1e-05
    )
    normalized_input = centered_input * reciprocal_deviation
    return (normalized_input, reciprocal_deviation, (normalized_input * gamma).astype(jnp.bfloat16))


def _attn_kernel(qkv_ref, do_ref, keep_ref, o_ref, dqkv_ref, *, scale, n, tq):
    qT = qkv_ref[0]
    kT = qkv_ref[1]
    vT = qkv_ref[2]
    doT = do_ref[...]
    keep = keep_ref[...] > 0.5
    d = qT.shape[0]
    dk_acc = jnp.zeros((d, n), jnp.float32)
    dv_acc = jnp.zeros((d, n), jnp.float32)
    k_rows = kT.T
    v_rows = vT.T
    for b in range(n // tq):
        cols = slice(b * tq, (b + 1) * tq)
        qT_b = qT[:, cols]
        doT_b = doT[:, cols]
        q_b = qT_b.T
        do_b = doT_b.T
        s = jnp.dot(q_b, kT, preferred_element_type=jnp.float32) * scale
        s = jnp.where(keep, s, -1e30)
        m = jnp.max(s, -1, keepdims=True)
        e = jnp.exp(s - m)
        l = jnp.sum(e, -1, keepdims=True)
        p = e * (1.0 / l)
        pb = p.astype(jnp.bfloat16)
        o_ref[:, cols] = (
            jnp.dot(pb, v_rows, preferred_element_type=jnp.float32).T.astype(o_ref.dtype)
        )
        dv_acc = dv_acc + jnp.dot(doT_b, pb, preferred_element_type=jnp.float32)
        dp = jnp.dot(do_b, vT, preferred_element_type=jnp.float32)
        rs = jnp.sum(dp * p, -1, keepdims=True)
        ds = (p * (dp - rs) * scale).astype(jnp.bfloat16)
        dqkv_ref[0, :, cols] = (
            jnp.dot(ds, k_rows, preferred_element_type=jnp.float32).T.astype(dqkv_ref.dtype)
        )
        dk_acc = dk_acc + jnp.dot(qT_b, ds, preferred_element_type=jnp.float32)
    dqkv_ref[1] = dk_acc.astype(dqkv_ref.dtype)
    dqkv_ref[2] = dv_acc.astype(dqkv_ref.dtype)


def fused_attention(qkvT, doT, keep_row, heads, first, count):
    _, c, n = qkvT.shape
    d = c // heads
    scale = d ** (-0.5)
    kernel = functools.partial(_attn_kernel, scale=scale, n=n, tq=TQ)
    flops = count * 6 * 2 * n * n * d
    return pl.pallas_call(
        kernel,
        grid=(count,),
        in_specs=[
            pl.BlockSpec((3, d, n), lambda h: (0, h + first, 0)),
            pl.BlockSpec((d, n), lambda h: (h + first, 0)),
            pl.BlockSpec((1, n), lambda h: (0, 0)),
        ],
        out_specs=[
            pl.BlockSpec((d, n), lambda h: (h, 0)),
            pl.BlockSpec((3, d, n), lambda h: (0, h, 0)),
        ],
        out_shape=[
            jax.ShapeDtypeStruct((count * d, n), jnp.bfloat16),
            jax.ShapeDtypeStruct((3, count * d, n), jnp.bfloat16),
        ],
        compiler_params=pltpu.CompilerParams(dimension_semantics=("arbitrary",)),
        cost_estimate=pl.CostEstimate(
            flops=flops, transcendentals=count * n * n, bytes_accessed=2 * 8 * count * d * n
        ),
    )(qkvT, doT, keep_row)


def to_all(array):
    size = lax.axis_size("gx") * lax.axis_size("gy")
    shaped = array.reshape(size, -1, array.shape[-1])
    moved = lax.all_to_all(shaped, ("gx", "gy"), split_axis=0, concat_axis=0, tiled=True)
    return moved.reshape(array.shape)


def device_sum(got):
    ones = jnp.ones((1, got.shape[0]), got.dtype)
    flat = jnp.dot(ones, got.reshape(got.shape[0], -1), preferred_element_type=jnp.float32)
    return flat.reshape((1,) + got.shape[1:])


def exchange(payload):
    return lax.all_to_all(payload, ("gx", "gy"), split_axis=0, concat_axis=0, tiled=True)


def half_grads(hidden_state, d_qkvT_half, attnT_half, gt):
    wq = lax.dot_general(
        hidden_state, d_qkvT_half.reshape(-1, d_qkvT_half.shape[-1]),
        (((0,), (1,)), ((), ())), preferred_element_type=jnp.float32,
    )
    wo = jnp.dot(attnT_half, gt, preferred_element_type=jnp.float32)
    return wq, wo


def block(features, valid, cotangent, gamma, w_qkv, w_out):
    rows, width = features.shape
    size = lax.axis_size("gx") * lax.axis_size("gy")
    nodes = rows * size
    inverse_root = float(nodes) ** (-0.5)
    half = HEADS // 2
    hw = width // 2
    per_dev = rows // size
    flag = jnp.zeros((rows, 128), jnp.bfloat16).at[:, 0].set(valid.astype(jnp.bfloat16))
    moved = to_all(jnp.concatenate([features, cotangent, flag], 1))
    input_rows = moved[:, :width]
    gt = moved[:, width : 2 * width]
    occupied = moved[:, 2 * width]
    normalized_input, reciprocal_deviation, hidden_state = layer_norm_apply(input_rows, gamma)
    qkvT = lax.dot_general(
        w_qkv, hidden_state, (((0,), (1,)), ((), ())), preferred_element_type=jnp.float32
    ).astype(jnp.bfloat16).reshape(3, width, rows)
    keep_row = occupied.astype(jnp.float32).reshape(1, rows)
    d_attnT = lax.dot_general(
        w_out, gt, (((1,), (1,)), ((), ())), preferred_element_type=jnp.float32
    ).astype(jnp.bfloat16)

    attn_a, dqkv_a = fused_attention(qkvT, d_attnT, keep_row, HEADS, 0, half)
    wq_a, wo_a = half_grads(hidden_state, dqkv_a, attn_a, gt)
    n_wq = wq_a.size
    pay_a = jnp.concatenate([wq_a.reshape(-1), wo_a.reshape(-1)]).reshape(size, -1, width)
    got_a = exchange(pay_a.astype(jnp.bfloat16))
    attn_b, dqkv_b = fused_attention(qkvT, d_attnT, keep_row, HEADS, half, half)
    mine_a = device_sum(got_a)
    attnT = jnp.concatenate([attn_a, attn_b], 0)
    y_val = (
        input_rows.astype(jnp.float32)
        + lax.dot_general(attnT, w_out, (((0,), (0,)), ((), ())), preferred_element_type=jnp.float32)
    ).astype(jnp.bfloat16)
    na = pay_a.shape[1]
    spread_a = jnp.broadcast_to(mine_a.astype(jnp.bfloat16), (size, na, width))
    back_a = exchange(
        jnp.concatenate([spread_a, y_val.reshape(size, per_dev, width)], 1)
    )
    total_a = back_a[:, :na].astype(jnp.float32).reshape(-1)
    y_plain = back_a[:, na:].reshape(rows, width)

    wq_b, wo_b = half_grads(hidden_state, dqkv_b, attn_b, gt)
    d_qkvT = jnp.concatenate([dqkv_a, dqkv_b], 1).reshape(3 * width, rows)
    hidden_gradient = lax.dot_general(
        d_qkvT, w_qkv, (((0,), (1,)), ((), ())), preferred_element_type=jnp.float32
    )
    shard_gamma = jnp.dot(
        jnp.ones((1, rows), jnp.float32),
        hidden_gradient * normalized_input,
        precision=lax.Precision.HIGHEST,
        preferred_element_type=jnp.float32,
    )[0]
    scaled_output = hidden_gradient * gamma
    norm_gradient = reciprocal_deviation * (
        scaled_output
        - jnp.mean(scaled_output, -1, keepdims=True)
        - normalized_input * jnp.mean(scaled_output * normalized_input, -1, keepdims=True)
    )
    d_x = (gt.astype(jnp.float32) + norm_gradient).astype(jnp.bfloat16)
    main_b = jnp.concatenate([wq_b.reshape(-1), wo_b.reshape(-1)]).reshape(size, -1, width)
    per = width // size
    side = jnp.zeros((size, 1, width), jnp.float32).at[:, 0, :per].set(
        shard_gamma.reshape(size, per)
    )
    pay_b = jnp.concatenate([main_b, side], 1)
    nb = pay_b.shape[1]
    payload = jnp.concatenate([d_x.reshape(size, per_dev, width), pay_b.astype(jnp.bfloat16)], 1)
    moved_b = exchange(payload)
    dx_plain = moved_b[:, :per_dev].reshape(rows, width)
    mine_b = device_sum(moved_b[:, per_dev:])
    total_b = exchange(jnp.broadcast_to(mine_b.astype(jnp.bfloat16), (size, nb, width)))
    total_b = total_b.astype(jnp.float32)
    gamma_total = total_b[:, -1, :per].reshape(width)
    flat_b = total_b[:, :-1, :].reshape(-1)

    def unpack(flat):
        wq = flat[:n_wq].reshape(width, 3, hw)
        wo = flat[n_wq:].reshape(hw, width)
        return wq, wo

    wq_ta, wo_ta = unpack(total_a)
    wq_tb, wo_tb = unpack(flat_b)
    total_wqkv = jnp.concatenate([wq_ta, wq_tb], 2).reshape(width, 3 * width)
    total_wout = jnp.concatenate([wo_ta, wo_tb], 0)
    return (
        y_plain,
        dx_plain,
        total_wqkv * inverse_root,
        total_wout * inverse_root,
        gamma_total * inverse_root,
    )


def solution(mesh):
    placed = (P(("gx", "gy"), None), P(("gx", "gy")), P(("gx", "gy"), None), P(), P(), P())
    return jax.shard_map(
        block,
        mesh=mesh,
        in_specs=placed,
        out_specs=(P(("gx", "gy"), None), P(("gx", "gy"), None), P(), P(), P()),
        check_vma=False,
    )
```

```python
import functools

import jax
import jax.numpy as jnp
from jax import lax
from jax.experimental import pallas as pl
from jax.experimental.pallas import tpu as pltpu
from jax.sharding import PartitionSpec as P

HEADS = 16
K = 1024
TQ = 512


def layer_norm_apply(input_rows, gamma):
    xf = input_rows.astype(jnp.float32)
    centered_input = xf - jnp.mean(xf, -1, keepdims=True)
    reciprocal_deviation = lax.rsqrt(
        jnp.mean(centered_input * centered_input, -1, keepdims=True) + 1e-05
    )
    normalized_input = centered_input * reciprocal_deviation
    return (normalized_input, reciprocal_deviation, (normalized_input * gamma).astype(jnp.bfloat16))


def _attn_kernel(qkv_ref, do_ref, keep_ref, o_ref, dqkv_ref, *, scale, n, tq, d, group):
    keep = keep_ref[...] > 0.5
    for g in range(group):
        rows = slice(g * d, (g + 1) * d)
        qT = qkv_ref[0, rows, :]
        kT = qkv_ref[1, rows, :]
        vT = qkv_ref[2, rows, :]
        doT = do_ref[rows, :]
        dk_acc = jnp.zeros((d, n), jnp.float32)
        dv_acc = jnp.zeros((d, n), jnp.float32)
        k_rows = kT.T
        v_rows = vT.T
        for b in range(n // tq):
            cols = slice(b * tq, (b + 1) * tq)
            qT_b = qT[:, cols]
            doT_b = doT[:, cols]
            q_b = qT_b.T
            do_b = doT_b.T
            s = jnp.dot(q_b, kT, preferred_element_type=jnp.float32) * scale
            s = jnp.where(keep, s, -1e30)
            m = jnp.max(s, -1, keepdims=True)
            e = jnp.exp(s - m)
            l = jnp.sum(e, -1, keepdims=True)
            p = e * (1.0 / l)
            pb = p.astype(jnp.bfloat16)
            o_ref[rows, cols] = (
                jnp.dot(pb, v_rows, preferred_element_type=jnp.float32).T.astype(o_ref.dtype)
            )
            dv_acc = dv_acc + jnp.dot(doT_b, pb, preferred_element_type=jnp.float32)
            dp = jnp.dot(do_b, vT, preferred_element_type=jnp.float32)
            rs = jnp.sum(dp * p, -1, keepdims=True)
            ds = (p * (dp - rs) * scale).astype(jnp.bfloat16)
            dqkv_ref[0, rows, cols] = (
                jnp.dot(ds, k_rows, preferred_element_type=jnp.float32).T.astype(dqkv_ref.dtype)
            )
            dk_acc = dk_acc + jnp.dot(qT_b, ds, preferred_element_type=jnp.float32)
        dqkv_ref[1, rows, :] = dk_acc.astype(dqkv_ref.dtype)
        dqkv_ref[2, rows, :] = dv_acc.astype(dqkv_ref.dtype)


def fused_attention(qkvT, doT, keep_row, heads):
    _, c, n = qkvT.shape
    d = c // heads
    scale = d ** (-0.5)
    group = 2
    kernel = functools.partial(_attn_kernel, scale=scale, n=n, tq=TQ, d=d, group=group)
    flops = heads * 6 * 2 * n * n * d
    return pl.pallas_call(
        kernel,
        grid=(heads // group,),
        in_specs=[
            pl.BlockSpec((3, group * d, n), lambda h: (0, h, 0)),
            pl.BlockSpec((group * d, n), lambda h: (h, 0)),
            pl.BlockSpec((1, n), lambda h: (0, 0)),
        ],
        out_specs=[
            pl.BlockSpec((group * d, n), lambda h: (h, 0)),
            pl.BlockSpec((3, group * d, n), lambda h: (0, h, 0)),
        ],
        out_shape=[
            jax.ShapeDtypeStruct((c, n), jnp.bfloat16),
            jax.ShapeDtypeStruct((3, c, n), jnp.bfloat16),
        ],
        compiler_params=pltpu.CompilerParams(dimension_semantics=("arbitrary",)),
        cost_estimate=pl.CostEstimate(
            flops=flops, transcendentals=heads * n * n, bytes_accessed=2 * 8 * c * n
        ),
    )(qkvT, doT, keep_row)


def to_all(array):
    size = lax.axis_size("gx") * lax.axis_size("gy")
    shaped = array.reshape(size, -1, array.shape[-1])
    moved = lax.all_to_all(shaped, ("gx", "gy"), split_axis=0, concat_axis=0, tiled=True)
    return moved.reshape(array.shape)


def sum_all(parts, scale):
    size = lax.axis_size("gx") * lax.axis_size("gy")
    matrix, vector = parts
    rows, cols = matrix.shape
    per = rows // size
    side = jnp.zeros((size, per, 128), jnp.float32).at[:, :, 0].set(vector.reshape(size, per))
    payload = jnp.concatenate([matrix.reshape(size, per, cols), side], 2)
    moved = lax.all_to_all(
        payload.astype(jnp.bfloat16), ("gx", "gy"), split_axis=0, concat_axis=0, tiled=True
    )
    ones = jnp.ones((1, size), jnp.bfloat16)
    mine = jnp.dot(ones, moved.reshape(size, -1), preferred_element_type=jnp.float32) * scale
    spread = jnp.broadcast_to(mine.astype(jnp.bfloat16).reshape((1,) + payload.shape[1:]), payload.shape)
    total = lax.all_to_all(
        spread, ("gx", "gy"), split_axis=0, concat_axis=0, tiled=True
    ).astype(jnp.float32)
    return total[:, :, :cols].reshape(rows, cols), total[:, :, cols].reshape(rows)


def shards(features, valid, cotangent, gamma, w_qkv, w_out):
    rows, width = features.shape
    nodes = rows * lax.axis_size("gx") * lax.axis_size("gy")
    inverse_root = float(nodes) ** (-0.5)
    flag = jnp.zeros((rows, 128), jnp.bfloat16).at[:, 0].set(valid.astype(jnp.bfloat16))
    moved = to_all(jnp.concatenate([features, cotangent, flag], 1))
    input_rows = moved[:, :width]
    gt = moved[:, width : 2 * width]
    occupied = moved[:, 2 * width]
    normalized_input, reciprocal_deviation, hidden_state = layer_norm_apply(input_rows, gamma)
    qkvT = lax.dot_general(
        w_qkv, hidden_state, (((0,), (1,)), ((), ())), preferred_element_type=jnp.float32
    ).astype(jnp.bfloat16)
    keep_row = occupied.astype(jnp.float32).reshape(1, rows)
    d_attnT = lax.dot_general(
        w_out, gt, (((1,), (1,)), ((), ())), preferred_element_type=jnp.float32
    ).astype(jnp.bfloat16)
    attnT, d_qkvT = fused_attention(qkvT.reshape(3, width, rows), d_attnT, keep_row, HEADS)
    d_qkvT = d_qkvT.reshape(3 * width, rows)
    y_val = (
        input_rows.astype(jnp.float32)
        + lax.dot_general(attnT, w_out, (((0,), (0,)), ((), ())), preferred_element_type=jnp.float32)
    ).astype(jnp.bfloat16)
    y_plain = to_all(y_val)
    local_wout = jnp.dot(attnT, gt, preferred_element_type=jnp.float32)
    local_wqkv = lax.dot_general(
        hidden_state, d_qkvT, (((0,), (1,)), ((), ())), preferred_element_type=jnp.float32
    )
    hidden_gradient = lax.dot_general(
        d_qkvT, w_qkv, (((0,), (1,)), ((), ())), preferred_element_type=jnp.float32
    )
    shard_gamma = jnp.dot(
        jnp.ones((1, rows), jnp.float32),
        hidden_gradient * normalized_input,
        precision=lax.Precision.HIGHEST,
        preferred_element_type=jnp.float32,
    )[0]
    scaled_output = hidden_gradient * gamma
    norm_gradient = reciprocal_deviation * (
        scaled_output
        - jnp.mean(scaled_output, -1, keepdims=True)
        - normalized_input * jnp.mean(scaled_output * normalized_input, -1, keepdims=True)
    )
    d_x = (gt.astype(jnp.float32) + norm_gradient).astype(jnp.bfloat16)
    total_w, total_gamma = sum_all(
        (jnp.concatenate([local_wqkv, local_wout], 1), shard_gamma), inverse_root
    )
    dx_plain = to_all(d_x)
    return (
        y_plain,
        dx_plain,
        total_w[:, : 3 * width],
        total_w[:, 3 * width :],
        total_gamma,
    )


def solution(mesh):
    placed = (P(("gx", "gy"), None), P(("gx", "gy")), P(("gx", "gy"), None), P(), P(), P())
    return jax.shard_map(
        shards,
        mesh=mesh,
        in_specs=placed,
        out_specs=(P(("gx", "gy"), None), P(("gx", "gy"), None), P(), P(), P()),
        check_vma=False,
    )
```

```python
import functools

import jax
import jax.numpy as jnp
from jax import lax
from jax.experimental import pallas as pl
from jax.experimental.pallas import tpu as pltpu
from jax.sharding import PartitionSpec as P


HEADS = 16
TQ = 512


def layer_norm_apply(input_rows, gamma):
    xf = input_rows.astype(jnp.float32)
    centered_input = xf - jnp.mean(xf, -1, keepdims=True)
    reciprocal_deviation = lax.rsqrt(
        jnp.mean(centered_input * centered_input, -1, keepdims=True) + 1e-05
    )
    normalized_input = centered_input * reciprocal_deviation
    return (normalized_input, reciprocal_deviation, (normalized_input * gamma).astype(jnp.bfloat16))


def _attn_kernel(qkv_ref, do_ref, keep_ref, o_ref, dqkv_ref, *, scale, n, tq, d, group):
    keep = keep_ref[...] > 0.5
    for g in range(group):
        rows = slice(g * d, (g + 1) * d)
        qT = qkv_ref[0, rows, :]
        kT = qkv_ref[1, rows, :]
        vT = qkv_ref[2, rows, :]
        doT = do_ref[rows, :]
        dk_acc = jnp.zeros((d, n), jnp.float32)
        dv_acc = jnp.zeros((d, n), jnp.float32)
        k_rows = kT.T
        v_rows = vT.T
        for b in range(n // tq):
            cols = slice(b * tq, (b + 1) * tq)
            qT_b = qT[:, cols]
            doT_b = doT[:, cols]
            q_b = qT_b.T
            do_b = doT_b.T
            s = jnp.dot(q_b, kT, preferred_element_type=jnp.float32) * scale
            s = jnp.where(keep, s, -1e30)
            m = jnp.max(s, -1, keepdims=True)
            e = jnp.exp(s - m)
            l = jnp.sum(e, -1, keepdims=True)
            p = e * (1.0 / l)
            pb = p.astype(jnp.bfloat16)
            o_ref[rows, cols] = (
                jnp.dot(pb, v_rows, preferred_element_type=jnp.float32).T.astype(o_ref.dtype)
            )
            dv_acc = dv_acc + jnp.dot(doT_b, pb, preferred_element_type=jnp.float32)
            dp = jnp.dot(do_b, vT, preferred_element_type=jnp.float32)
            rs = jnp.sum(dp * p, -1, keepdims=True)
            ds = (p * (dp - rs) * scale).astype(jnp.bfloat16)
            dqkv_ref[0, rows, cols] = (
                jnp.dot(ds, k_rows, preferred_element_type=jnp.float32).T.astype(dqkv_ref.dtype)
            )
            dk_acc = dk_acc + jnp.dot(qT_b, ds, preferred_element_type=jnp.float32)
        dqkv_ref[1, rows, :] = dk_acc.astype(dqkv_ref.dtype)
        dqkv_ref[2, rows, :] = dv_acc.astype(dqkv_ref.dtype)


def fused_attention(qkvT, doT, keep_row, heads):
    _, c, n = qkvT.shape
    d = c // heads
    scale = d ** (-0.5)
    group = 2
    kernel = functools.partial(_attn_kernel, scale=scale, n=n, tq=TQ, d=d, group=group)
    flops = heads * 6 * 2 * n * n * d
    return pl.pallas_call(
        kernel,
        grid=(heads // group,),
        in_specs=[
            pl.BlockSpec((3, group * d, n), lambda h: (0, h, 0)),
            pl.BlockSpec((group * d, n), lambda h: (h, 0)),
            pl.BlockSpec((1, n), lambda h: (0, 0)),
        ],
        out_specs=[
            pl.BlockSpec((group * d, n), lambda h: (h, 0)),
            pl.BlockSpec((3, group * d, n), lambda h: (0, h, 0)),
        ],
        out_shape=[
            jax.ShapeDtypeStruct((c, n), jnp.bfloat16),
            jax.ShapeDtypeStruct((3, c, n), jnp.bfloat16),
        ],
        compiler_params=pltpu.CompilerParams(dimension_semantics=("arbitrary",)),
        cost_estimate=pl.CostEstimate(
            flops=flops, transcendentals=heads * n * n, bytes_accessed=2 * 8 * c * n
        ),
    )(qkvT, doT, keep_row)


def to_all(array):
    size = lax.axis_size("gx") * lax.axis_size("gy")
    shaped = array.reshape(size, -1, array.shape[-1])
    moved = lax.all_to_all(shaped, ("gx", "gy"), split_axis=0, concat_axis=0, tiled=True)
    return moved.reshape(array.shape)


def block(features, valid, cotangent, gamma, w_qkv, w_out):
    rows, width = features.shape
    nodes = rows * lax.axis_size("gx") * lax.axis_size("gy")
    inverse_root = float(nodes) ** (-0.5)
    flag = jnp.zeros((rows, 128), jnp.bfloat16).at[:, 0].set(valid.astype(jnp.bfloat16))
    moved = to_all(jnp.concatenate([features, cotangent, flag], 1))
    input_rows = moved[:, :width]
    gt = moved[:, width : 2 * width]
    occupied = moved[:, 2 * width]
    normalized_input, reciprocal_deviation, hidden_state = layer_norm_apply(input_rows, gamma)
    qkvT = lax.dot_general(
        w_qkv, hidden_state, (((0,), (1,)), ((), ())), preferred_element_type=jnp.float32
    ).astype(jnp.bfloat16)
    keep_row = occupied.astype(jnp.float32).reshape(1, rows)
    d_attnT = lax.dot_general(
        w_out, gt, (((1,), (1,)), ((), ())), preferred_element_type=jnp.float32
    ).astype(jnp.bfloat16)
    attnT, d_qkvT = fused_attention(qkvT.reshape(3, width, rows), d_attnT, keep_row, HEADS)
    d_qkvT = d_qkvT.reshape(3 * width, rows)
    size = lax.axis_size("gx") * lax.axis_size("gy")
    per_dev = rows // size
    y_val = (
        input_rows.astype(jnp.float32)
        + lax.dot_general(
            attnT, w_out, (((0,), (0,)), ((), ())), preferred_element_type=jnp.float32
        )
    ).astype(jnp.bfloat16)
    y_plain = lax.all_to_all(
        y_val.reshape(size, per_dev, width), ("gx", "gy"), split_axis=0, concat_axis=0,
        tiled=True,
    ).reshape(rows, width)
    local_wout = jnp.dot(attnT, gt, preferred_element_type=jnp.float32)
    local_wqkv = lax.dot_general(
        hidden_state, d_qkvT, (((0,), (1,)), ((), ())), preferred_element_type=jnp.float32
    )
    hidden_gradient = lax.dot_general(
        d_qkvT, w_qkv, (((0,), (1,)), ((), ())), preferred_element_type=jnp.float32
    )
    shard_gamma = jnp.dot(
        jnp.ones((1, rows), jnp.float32),
        hidden_gradient * normalized_input,
        precision=lax.Precision.HIGHEST,
        preferred_element_type=jnp.float32,
    )[0]
    matrix = jnp.concatenate([local_wqkv, local_wout], 1)
    cols = matrix.shape[1]
    per = width // size
    side = jnp.zeros((size, per, 128), jnp.float32).at[:, :, 0].set(shard_gamma.reshape(size, per))
    payload = jnp.concatenate([matrix.reshape(size, per, cols), side], 2)
    moved = lax.all_to_all(
        payload.astype(jnp.bfloat16), ("gx", "gy"), split_axis=0, concat_axis=0, tiled=True
    )
    scaled_output = hidden_gradient * gamma
    norm_gradient = reciprocal_deviation * (
        scaled_output
        - jnp.mean(scaled_output, -1, keepdims=True)
        - normalized_input * jnp.mean(scaled_output * normalized_input, -1, keepdims=True)
    )
    d_x = (gt.astype(jnp.float32) + norm_gradient).astype(jnp.bfloat16)
    back = lax.all_to_all(
        d_x.reshape(size, per_dev, width), ("gx", "gy"), split_axis=0, concat_axis=0,
        tiled=True,
    )
    dx_plain = back.reshape(rows, width)
    ones = jnp.ones((1, size), jnp.bfloat16)
    mine = jnp.dot(ones, moved.reshape(size, -1), preferred_element_type=jnp.float32)
    mine = mine * inverse_root
    spread = jnp.broadcast_to(
        mine.astype(jnp.bfloat16).reshape((1,) + payload.shape[1:]), payload.shape
    )
    total = lax.all_to_all(
        spread, ("gx", "gy"), split_axis=0, concat_axis=0, tiled=True
    ).astype(jnp.float32)
    total_w = total[:, :, :cols].reshape(width, cols)
    total_gamma = total[:, :, cols].reshape(width)
    return (
        y_plain,
        dx_plain,
        total_w[:, : 3 * width],
        total_w[:, 3 * width :],
        total_gamma,
    )


def solution(mesh):
    placed = (P(("gx", "gy"), None), P(("gx", "gy")), P(("gx", "gy"), None), P(), P(), P())
    return jax.shard_map(
        block,
        mesh=mesh,
        in_specs=placed,
        out_specs=(P(("gx", "gy"), None), P(("gx", "gy"), None), P(), P(), P()),
        check_vma=False,
    )
```

```python
import functools

import jax
import jax.numpy as jnp
from jax import lax
from jax.experimental import pallas as pl
from jax.experimental.pallas import tpu as pltpu
from jax.sharding import PartitionSpec as P


HEADS = 16
TQ = 512


def layer_norm_apply(input_rows, gamma):
    xf = input_rows.astype(jnp.float32)
    centered_input = xf - jnp.mean(xf, -1, keepdims=True)
    reciprocal_deviation = lax.rsqrt(
        jnp.mean(centered_input * centered_input, -1, keepdims=True) + 1e-05
    )
    normalized_input = centered_input * reciprocal_deviation
    return (normalized_input, reciprocal_deviation, (normalized_input * gamma).astype(jnp.bfloat16))


def _attn_kernel(qkv_ref, do_ref, keep_ref, o_ref, dqkv_ref, *, scale, n, tq, d, group):
    keep = keep_ref[...] > 0.5
    for g in range(group):
        rows = slice(g * d, (g + 1) * d)
        qT = qkv_ref[0, rows, :]
        kT = qkv_ref[1, rows, :]
        vT = qkv_ref[2, rows, :]
        doT = do_ref[rows, :]
        dk_acc = jnp.zeros((d, n), jnp.float32)
        dv_acc = jnp.zeros((d, n), jnp.float32)
        k_rows = kT.T
        v_rows = vT.T
        for b in range(n // tq):
            cols = slice(b * tq, (b + 1) * tq)
            qT_b = qT[:, cols]
            doT_b = doT[:, cols]
            q_b = qT_b.T
            do_b = doT_b.T
            s = jnp.dot(q_b, kT, preferred_element_type=jnp.float32) * scale
            s = jnp.where(keep, s, -1e30)
            m = jnp.max(s, -1, keepdims=True)
            e = jnp.exp(s - m)
            l = jnp.sum(e, -1, keepdims=True)
            p = e * (1.0 / l)
            pb = p.astype(jnp.bfloat16)
            o_ref[rows, cols] = (
                jnp.dot(pb, v_rows, preferred_element_type=jnp.float32).T.astype(o_ref.dtype)
            )
            dv_acc = dv_acc + jnp.dot(doT_b, pb, preferred_element_type=jnp.float32)
            dp = jnp.dot(do_b, vT, preferred_element_type=jnp.float32)
            rs = jnp.sum(dp * p, -1, keepdims=True)
            ds = (p * (dp - rs) * scale).astype(jnp.bfloat16)
            dqkv_ref[0, rows, cols] = (
                jnp.dot(ds, k_rows, preferred_element_type=jnp.float32).T.astype(dqkv_ref.dtype)
            )
            dk_acc = dk_acc + jnp.dot(qT_b, ds, preferred_element_type=jnp.float32)
        dqkv_ref[1, rows, :] = dk_acc.astype(dqkv_ref.dtype)
        dqkv_ref[2, rows, :] = dv_acc.astype(dqkv_ref.dtype)


def fused_attention(qkvT, doT, keep_row, heads):
    _, c, n = qkvT.shape
    d = c // heads
    scale = d ** (-0.5)
    group = 4
    kernel = functools.partial(_attn_kernel, scale=scale, n=n, tq=TQ, d=d, group=group)
    flops = heads * 6 * 2 * n * n * d
    return pl.pallas_call(
        kernel,
        grid=(heads // group,),
        in_specs=[
            pl.BlockSpec((3, group * d, n), lambda h: (0, h, 0)),
            pl.BlockSpec((group * d, n), lambda h: (h, 0)),
            pl.BlockSpec((1, n), lambda h: (0, 0)),
        ],
        out_specs=[
            pl.BlockSpec((group * d, n), lambda h: (h, 0)),
            pl.BlockSpec((3, group * d, n), lambda h: (0, h, 0)),
        ],
        out_shape=[
            jax.ShapeDtypeStruct((c, n), jnp.bfloat16),
            jax.ShapeDtypeStruct((3, c, n), jnp.bfloat16),
        ],
        compiler_params=pltpu.CompilerParams(dimension_semantics=("arbitrary",)),
        cost_estimate=pl.CostEstimate(
            flops=flops, transcendentals=heads * n * n, bytes_accessed=2 * 8 * c * n
        ),
    )(qkvT, doT, keep_row)


def to_all(array):
    size = lax.axis_size("gx") * lax.axis_size("gy")
    shaped = array.reshape(size, -1, array.shape[-1])
    moved = lax.all_to_all(shaped, ("gx", "gy"), split_axis=0, concat_axis=0, tiled=True)
    return moved.reshape(array.shape)


def block(features, valid, cotangent, gamma, w_qkv, w_out):
    rows, width = features.shape
    nodes = rows * lax.axis_size("gx") * lax.axis_size("gy")
    inverse_root = float(nodes) ** (-0.5)
    flag = jnp.zeros((rows, 128), jnp.bfloat16).at[:, 0].set(valid.astype(jnp.bfloat16))
    moved = to_all(jnp.concatenate([features, cotangent, flag], 1))
    input_rows = moved[:, :width]
    gt = moved[:, width : 2 * width]
    occupied = moved[:, 2 * width]
    normalized_input, reciprocal_deviation, hidden_state = layer_norm_apply(input_rows, gamma)
    qkvT = lax.dot_general(
        w_qkv, hidden_state, (((0,), (1,)), ((), ())), preferred_element_type=jnp.float32
    ).astype(jnp.bfloat16)
    keep_row = occupied.astype(jnp.float32).reshape(1, rows)
    d_attnT = lax.dot_general(
        w_out, gt, (((1,), (1,)), ((), ())), preferred_element_type=jnp.float32
    ).astype(jnp.bfloat16)
    attnT, d_qkvT = fused_attention(qkvT.reshape(3, width, rows), d_attnT, keep_row, HEADS)
    d_qkvT = d_qkvT.reshape(3 * width, rows)
    local_wout = jnp.dot(attnT, gt, preferred_element_type=jnp.float32)
    local_wqkv = lax.dot_general(
        hidden_state, d_qkvT, (((0,), (1,)), ((), ())), preferred_element_type=jnp.float32
    )
    hidden_gradient = lax.dot_general(
        d_qkvT, w_qkv, (((0,), (1,)), ((), ())), preferred_element_type=jnp.float32
    )
    shard_gamma = jnp.dot(
        jnp.ones((1, rows), jnp.float32),
        hidden_gradient * normalized_input,
        precision=lax.Precision.HIGHEST,
        preferred_element_type=jnp.float32,
    )[0]
    size = lax.axis_size("gx") * lax.axis_size("gy")
    matrix = jnp.concatenate([local_wqkv, local_wout], 1)
    cols = matrix.shape[1]
    per = width // size
    side = jnp.zeros((size, per, 128), jnp.float32).at[:, :, 0].set(shard_gamma.reshape(size, per))
    payload = jnp.concatenate([matrix.reshape(size, per, cols), side], 2)
    moved = lax.all_to_all(
        payload.astype(jnp.bfloat16), ("gx", "gy"), split_axis=0, concat_axis=0, tiled=True
    )
    y_val = (
        input_rows.astype(jnp.float32)
        + lax.dot_general(
            attnT, w_out, (((0,), (0,)), ((), ())), preferred_element_type=jnp.float32
        )
    ).astype(jnp.bfloat16)
    scaled_output = hidden_gradient * gamma
    norm_gradient = reciprocal_deviation * (
        scaled_output
        - jnp.mean(scaled_output, -1, keepdims=True)
        - normalized_input * jnp.mean(scaled_output * normalized_input, -1, keepdims=True)
    )
    d_x = (gt.astype(jnp.float32) + norm_gradient).astype(jnp.bfloat16)
    per_dev = rows // size
    both = jnp.concatenate(
        [d_x.reshape(size, per_dev, width), y_val.reshape(size, per_dev, width)], 1
    )
    back = lax.all_to_all(both, ("gx", "gy"), split_axis=0, concat_axis=0, tiled=True)
    dx_plain = back[:, :per_dev].reshape(rows, width)
    y_plain = back[:, per_dev:].reshape(rows, width)
    ones = jnp.ones((1, size), jnp.bfloat16)
    mine = jnp.dot(ones, moved.reshape(size, -1), preferred_element_type=jnp.float32)
    mine = mine * inverse_root
    spread = jnp.broadcast_to(
        mine.astype(jnp.bfloat16).reshape((1,) + payload.shape[1:]), payload.shape
    )
    total = lax.all_to_all(
        spread, ("gx", "gy"), split_axis=0, concat_axis=0, tiled=True
    ).astype(jnp.float32)
    total_w = total[:, :, :cols].reshape(width, cols)
    total_gamma = total[:, :, cols].reshape(width)
    return (
        y_plain,
        dx_plain,
        total_w[:, : 3 * width],
        total_w[:, 3 * width :],
        total_gamma,
    )


def solution(mesh):
    placed = (P(("gx", "gy"), None), P(("gx", "gy")), P(("gx", "gy"), None), P(), P(), P())
    return jax.shard_map(
        block,
        mesh=mesh,
        in_specs=placed,
        out_specs=(P(("gx", "gy"), None), P(("gx", "gy"), None), P(), P(), P()),
        check_vma=False,
    )
```
